512 devices in a mesh: row: 16 (over z, core), col: 32 (over x, y).
Axes of the slice: x: 4, y: 8, z: 8, core: 2. Of those that a mesh axis runs over, the one named last changes fastest.
Arguments:
- pool: float32 [131072, 256], P(('row', 'col')), may hold values from -12 to 12
- row_pick: int32 [65536], replicated, may hold values from 0 to 8191, as said below
- length_scale: float32 [256], replicated, may hold values from 12 to 48
- panel_tile: int32 [1], replicated, may hold values from 0 to 959
Outputs:
- schur: float32 [65536, 4096], P('row', 'col')
- row_panel: float32 [65536, 64], P('row')
The draws below stay inside these ranges and needn't reach their ends.
Inputs may be any that keep to these rules, and one draw needn't show every extreme that they name: `row_pick`: entry m indexes the 8192 pixels of tile-grid row m // 4096; entries of one tile-grid row are distinct, at most 160 of them lie in the 256 pixels of one device, and exactly 160 do for some device of each tile-grid row.
All inputs are finite; a program needn't handle non-finite values.
Results may differ from the reference program's by a relative error of at most 0.0003.
Values sent between devices are 32-bit elements; how exact they have to be, the bound alone decides.
No kernel may reach another device: no remote copies, remote signals or barrier semaphores. Data moves between devices by JAX's collectives and lax.ppermute only.
A program may use at most 64 MiB of HBM per device.

```python
import math
import jax
import jax.numpy as jnp
from jax import lax

F = 256
TB = 64
WT = 2
POOL = 256
CAP = 160
RLOC = 4096
M = 65536
NT = 1024
WIN = 4096
NPIX = 131072
N_ROW = 16
N_COL = 32


def draw_pool(key, part):
    key_scale, key_base = jax.random.split(jax.random.fold_in(key, 11))
    scales = jnp.exp(jax.random.uniform(key_scale, (NPIX, 1), jnp.float32, jnp.log(0.5), jnp.log(2.0)))
    base = jnp.clip(jax.random.normal(key_base, (NPIX, F), jnp.float32), -6.0, 6.0)
    return scales * base


def pick_group(group_key):
    key_full, key_rank, key_order, key_shuffle = jax.random.split(group_key, 4)
    total = N_COL * POOL
    full_device = jax.random.randint(key_full, (), 0, N_COL)
    perms = jax.vmap(lambda inner: jax.random.permutation(inner, POOL))(jax.random.split(key_rank, N_COL))
    ranks = jnp.argsort(perms, axis=1, stable=True).reshape(-1)
    order = jax.random.permutation(key_order, total)
    position = jnp.argsort(order, stable=True)
    slots = jnp.arange(total)
    device = slots // POOL
    usable = ranks < CAP
    score = jnp.where(usable & (device == full_device), position, jnp.where(usable, total + position, 2 * total + position))
    chosen = jnp.argsort(score, stable=True)[:RLOC]
    shuffle = jax.random.permutation(key_shuffle, RLOC)
    return chosen[shuffle].astype(jnp.int32)


def draw_row_pick(key, part):
    keys = jax.random.split(jax.random.fold_in(key, 7), N_ROW)
    return jax.vmap(pick_group)(keys).reshape(-1).astype(jnp.int32)


def setup_inputs(seed: int = 0) -> dict:
    key_list = jax.random.split(jax.random.key(seed), 5)
    return {
        "pool": draw_pool(jax.random.fold_in(key_list[4], 71), 0),
        "row_pick": draw_row_pick(jax.random.fold_in(key_list[4], 71), 0),
        "length_scale": jnp.clip(jnp.exp(jax.random.uniform(key_list[2], (F,), jnp.float32, math.log(12.0), math.log(48.0))), 12.0, 48.0),
        "panel_tile": jax.random.randint(key_list[3], (1,), 0, NT - N_COL * WT).astype(jnp.int32),
    }


noise_level = 0.1
root_five = 5.0 ** 0.5

def kernel(left, right, left_index, right_index):
    left_sq = lax.optimization_barrier(jnp.sum(left * left, axis=1))
    right_sq = lax.optimization_barrier(jnp.sum(right * right, axis=1))
    cross = jnp.dot(left.astype(jnp.float32), right.T.astype(jnp.float32), precision=lax.Precision.HIGHEST, preferred_element_type=jnp.float32)
    dist_sq = jnp.maximum(left_sq[:, None] + right_sq[None, :] - 2.0 * cross, 0.0)
    radius = jnp.sqrt(dist_sq)
    value = (1.0 + root_five * radius + 5.0 / 3.0 * dist_sq) * jnp.exp(-root_five * radius)
    same = (left_index[:, None] == right_index[None, :]).astype(value.dtype)
    return value + noise_level * same

def panel_solve(factor, block):
    return lax.linalg.triangular_solve(factor, block, left_side=False, lower=True, transpose_a=True)

def reference(pool, row_pick, length_scale, panel_tile):
    positions = jnp.arange(M)
    group = positions // RLOC
    features = jnp.take(pool, group * (N_COL * POOL) + row_pick, axis=0)
    scaled = features * (1.0 / length_scale)
    local = positions % RLOC
    row_global = (local // TB * N_ROW + group) * TB + local % TB
    panel = panel_tile[0]
    start = (panel % N_ROW * RLOC + panel // N_ROW * TB).astype(jnp.int32)
    scaled_panel = lax.dynamic_slice_in_dim(scaled, start, TB)
    panel_global = panel * TB + jnp.arange(TB)
    column_pos = jnp.arange(WIN)
    column = column_pos // (WT * TB)
    inner = column_pos % (WT * TB)
    tile = panel + 1 + jnp.mod(column - panel - 1, N_COL) + N_COL * (inner // TB)
    offset = inner % TB
    col_source = tile % N_ROW * RLOC + tile // N_ROW * TB + offset
    scaled_cols = jnp.take(scaled, col_source, axis=0)
    col_global = tile * TB + offset
    factor = jnp.linalg.cholesky(kernel(scaled_panel, scaled_panel, panel_global, panel_global))
    row_panel = panel_solve(factor, kernel(scaled, scaled_panel, row_global, panel_global))
    col_panel = panel_solve(factor, kernel(scaled_cols, scaled_panel, col_global, panel_global))

    def block(index):
        begin = (index * RLOC).astype(jnp.int32)
        rows = lax.dynamic_slice_in_dim(scaled, begin, RLOC)
        rows_global = lax.dynamic_slice_in_dim(row_global, begin, RLOC)
        rows_panel = lax.dynamic_slice_in_dim(row_panel, begin, RLOC)
        update = jnp.dot(rows_panel.astype(jnp.float32), col_panel.T.astype(jnp.float32), precision=lax.Precision.HIGHEST, preferred_element_type=jnp.float32)
        return kernel(rows, scaled_cols, rows_global, col_global) - update
    schur = lax.map(block, jnp.arange(N_ROW)).reshape(M, WIN)
    return (schur, row_panel)
```

```python
import jax
import jax.numpy as jnp
from jax import lax
from jax.sharding import PartitionSpec as P

TB = 64
WT = 2


noise_level = 0.1
root_five = 5.0**0.5


def broadcast_rows(x, root, rows_count):
    dist = jnp.mod(lax.axis_index("row") - root, rows_count)
    step = 1
    while step < rows_count:
        perm = [(i, (i + step) % rows_count) for i in range(rows_count)]
        got = lax.ppermute(x, "row", perm)
        x = jnp.where((dist >= step) & (dist < 2 * step), got, x)
        step *= 2
    return x


def window_perm(rows_count, cols_count):
    pairs = []
    for g in range(rows_count):
        for c2 in range(cols_count):
            r = c2 % rows_count
            c = g + rows_count * (c2 // rows_count)
            pairs.append((g * cols_count + c2, r * cols_count + c))
    return pairs


def kernel(left, right, left_index, right_index):
    left_sq = jnp.sum(left * left, axis=1)
    right_sq = jnp.sum(right * right, axis=1)
    cross = jnp.dot(
        left, right.T, precision=lax.Precision.HIGHEST, preferred_element_type=jnp.float32
    )
    dist_sq = jnp.maximum(left_sq[:, None] + right_sq[None, :] - 2.0 * cross, 0.0)
    radius = jnp.sqrt(dist_sq)
    value = (1.0 + root_five * radius + 5.0 / 3.0 * dist_sq) * jnp.exp(-root_five * radius)
    same = (left_index[:, None] == right_index[None, :]).astype(value.dtype)
    return value + noise_level * same


def panel_solve(factor, block):
    return lax.linalg.triangular_solve(factor, block, left_side=False, lower=True, transpose_a=True)


def body(pool, row_pick, length_scale, panel_tile):
    rows_count = lax.axis_size("row")
    cols_count = lax.axis_size("col")
    my_row = lax.axis_index("row")
    my_col = lax.axis_index("col")
    total_rows = row_pick.shape[0]
    local_rows = total_rows // rows_count
    my_pick = lax.dynamic_slice_in_dim(row_pick, my_row * local_rows, local_rows)
    gathered = lax.all_gather(pool, "col", axis=0, tiled=True)
    features = jnp.take(gathered, my_pick, axis=0)
    panel = panel_tile[0]
    tiles = panel + 1 + jnp.mod(my_col - panel - 1, cols_count) + cols_count * jnp.arange(WT)
    served = my_row + rows_count * (my_col // rows_count)
    served_tiles = panel + 1 + jnp.mod(served - panel - 1, cols_count) + cols_count * jnp.arange(WT)
    local_tiles = served_tiles // rows_count
    col_source = (local_tiles[:, None] * TB + jnp.arange(TB)[None, :]).reshape(-1)
    col_local = jnp.take(features, col_source, axis=0)
    col_feats = lax.ppermute(col_local, ("row", "col"), window_perm(rows_count, cols_count))
    panel_row = panel % rows_count
    panel_local = panel // rows_count
    panel_rows = lax.dynamic_slice_in_dim(features, panel_local * TB, TB)
    panel_feats = broadcast_rows(panel_rows, panel_row, rows_count)
    inverse_scale = 1.0 / length_scale
    scaled_rows = features * inverse_scale
    scaled_cols = col_feats * inverse_scale
    scaled_panel = panel_feats * inverse_scale
    local_index = jnp.arange(local_rows)
    row_global = (local_index // TB * rows_count + my_row) * TB + local_index % TB
    col_global = (tiles[:, None] * TB + jnp.arange(TB)[None, :]).reshape(-1)
    panel_global = panel * TB + jnp.arange(TB)
    factor = jnp.linalg.cholesky(kernel(scaled_panel, scaled_panel, panel_global, panel_global))
    row_panel = panel_solve(factor, kernel(scaled_rows, scaled_panel, row_global, panel_global))
    col_panel = panel_solve(factor, kernel(scaled_cols, scaled_panel, col_global, panel_global))
    update = jnp.dot(
        row_panel, col_panel.T, precision=lax.Precision.HIGHEST, preferred_element_type=jnp.float32
    )
    schur = kernel(scaled_rows, scaled_cols, row_global, col_global) - update
    return (schur, row_panel)


def solution(mesh):
    in_specs = (P(("row", "col"), None), P(), P(), P())
    out_specs = (P("row", "col"), P("row", None))
    return jax.shard_map(body, mesh=mesh, in_specs=in_specs, out_specs=out_specs, check_vma=False)
```

```python
import jax
import jax.numpy as jnp
from jax import lax
from jax.sharding import PartitionSpec as P

TB = 64
WT = 2
CAP = 160


noise_level = 0.1
root_five = 5.0**0.5


def broadcast_rows(x, root, rows_count, radix=4):
    dist = jnp.mod(lax.axis_index("row") - root, rows_count)
    step = 1
    while step < rows_count:
        new = x
        for k in range(1, radix):
            shift = k * step
            if shift >= rows_count:
                break
            perm = [(i, (i + shift) % rows_count) for i in range(rows_count)]
            got = lax.ppermute(x, "row", perm)
            new = jnp.where((dist >= shift) & (dist < shift + step), got, new)
        x = new
        step *= radix
    return x


def window_perm(rows_count, cols_count):
    pairs = []
    for g in range(rows_count):
        for c2 in range(cols_count):
            r = c2 % rows_count
            c = g + rows_count * (c2 // rows_count)
            pairs.append((g * cols_count + c2, r * cols_count + c))
    return pairs


def kernel(left, right, left_index, right_index):
    left_sq = jnp.sum(left * left, axis=1)
    right_sq = jnp.sum(right * right, axis=1)
    cross = jnp.dot(
        left, right.T, precision=lax.Precision.HIGHEST, preferred_element_type=jnp.float32
    )
    dist_sq = jnp.maximum(left_sq[:, None] + right_sq[None, :] - 2.0 * cross, 0.0)
    radius = jnp.sqrt(dist_sq)
    value = (1.0 + root_five * radius + 5.0 / 3.0 * dist_sq) * jnp.exp(-root_five * radius)
    same = (left_index[:, None] == right_index[None, :]).astype(value.dtype)
    return value + noise_level * same


def panel_solve(factor, block):
    return lax.linalg.triangular_solve(factor, block, left_side=False, lower=True, transpose_a=True)


def body(pool, row_pick, length_scale, panel_tile):
    rows_count = lax.axis_size("row")
    cols_count = lax.axis_size("col")
    my_row = lax.axis_index("row")
    my_col = lax.axis_index("col")
    total_rows = row_pick.shape[0]
    local_rows = total_rows // rows_count
    my_pick = lax.dynamic_slice_in_dim(row_pick, my_row * local_rows, local_rows)
    pool_rows = pool.shape[0]
    group_pixels = pool_rows * cols_count
    picked = jnp.zeros((group_pixels,), jnp.int32).at[my_pick].set(1, unique_indices=True)
    counts = jnp.cumsum(picked.reshape(cols_count, pool_rows), axis=1)
    mine = lax.dynamic_index_in_dim(counts, my_col, axis=0, keepdims=False)
    slots = jnp.arange(CAP, dtype=jnp.int32)
    local_idx = jnp.sum((mine[None, :] <= slots[:, None]).astype(jnp.int32), axis=1)
    compact = jnp.take(pool, jnp.minimum(local_idx, pool_rows - 1), axis=0)
    gathered = lax.all_gather(compact, "col", axis=0, tiled=True)
    slot_of = (counts - 1).reshape(-1)
    pick_idx = my_pick // pool_rows * CAP + jnp.take(slot_of, my_pick)
    features = jnp.take(gathered, pick_idx, axis=0)
    panel = panel_tile[0]
    tiles = panel + 1 + jnp.mod(my_col - panel - 1, cols_count) + cols_count * jnp.arange(WT)
    served = my_row + rows_count * (my_col // rows_count)
    served_tiles = panel + 1 + jnp.mod(served - panel - 1, cols_count) + cols_count * jnp.arange(WT)
    local_tiles = served_tiles // rows_count
    col_source = (local_tiles[:, None] * TB + jnp.arange(TB)[None, :]).reshape(-1)
    col_local = jnp.take(gathered, jnp.take(pick_idx, col_source), axis=0)
    col_feats = lax.ppermute(col_local, ("row", "col"), window_perm(rows_count, cols_count))
    panel_row = panel % rows_count
    panel_local = panel // rows_count
    panel_rows = jnp.take(gathered, lax.dynamic_slice_in_dim(pick_idx, panel_local * TB, TB), axis=0)
    panel_feats = broadcast_rows(panel_rows, panel_row, rows_count)
    inverse_scale = 1.0 / length_scale
    scaled_rows = features * inverse_scale
    scaled_cols = col_feats * inverse_scale
    scaled_panel = panel_feats * inverse_scale
    local_index = jnp.arange(local_rows)
    row_global = (local_index // TB * rows_count + my_row) * TB + local_index % TB
    col_global = (tiles[:, None] * TB + jnp.arange(TB)[None, :]).reshape(-1)
    panel_global = panel * TB + jnp.arange(TB)
    factor = jnp.linalg.cholesky(kernel(scaled_panel, scaled_panel, panel_global, panel_global))
    row_panel = panel_solve(factor, kernel(scaled_rows, scaled_panel, row_global, panel_global))
    col_panel = panel_solve(factor, kernel(scaled_cols, scaled_panel, col_global, panel_global))
    update = jnp.dot(
        row_panel, col_panel.T, precision=lax.Precision.HIGHEST, preferred_element_type=jnp.float32
    )
    schur = kernel(scaled_rows, scaled_cols, row_global, col_global) - update
    return (schur, row_panel)


def solution(mesh):
    in_specs = (P(("row", "col"), None), P(), P(), P())
    out_specs = (P("row", "col"), P("row", None))
    return jax.shard_map(body, mesh=mesh, in_specs=in_specs, out_specs=out_specs, check_vma=False)
```

```python
import jax
import jax.numpy as jnp
from jax import lax
from jax.sharding import PartitionSpec as P

TB = 64
WT = 2
CAP = 160


noise_level = 0.1
root_five = 5.0**0.5


def broadcast_rows(x, root, rows_count, radix=4):
    dist = jnp.mod(lax.axis_index("row") - root, rows_count)
    step = 1
    while step < rows_count:
        new = x
        for k in range(1, radix):
            shift = k * step
            if shift >= rows_count:
                break
            perm = [(i, (i + shift) % rows_count) for i in range(rows_count)]
            got = lax.ppermute(x, "row", perm)
            new = jnp.where((dist >= shift) & (dist < shift + step), got, new)
        x = new
        step *= radix
    return x


def window_perm(rows_count, cols_count):
    pairs = []
    for g in range(rows_count):
        for c2 in range(cols_count):
            r = c2 % rows_count
            c = g + rows_count * (c2 // rows_count)
            pairs.append((g * cols_count + c2, r * cols_count + c))
    return pairs


def kernel(left, right, left_index, right_index):
    left_sq = jnp.sum(left * left, axis=1)
    right_sq = jnp.sum(right * right, axis=1)
    cross = jnp.dot(
        left, right.T, precision=lax.Precision.HIGHEST, preferred_element_type=jnp.float32
    )
    dist_sq = jnp.maximum(left_sq[:, None] + right_sq[None, :] - 2.0 * cross, 0.0)
    radius = jnp.sqrt(dist_sq)
    value = (1.0 + root_five * radius + 5.0 / 3.0 * dist_sq) * jnp.exp(-root_five * radius)
    same = (left_index[:, None] == right_index[None, :]).astype(value.dtype)
    return value + noise_level * same


def panel_solve(factor, block):
    return lax.linalg.triangular_solve(factor, block, left_side=False, lower=True, transpose_a=True)


def body(pool, row_pick, length_scale, panel_tile):
    rows_count = lax.axis_size("row")
    cols_count = lax.axis_size("col")
    my_row = lax.axis_index("row")
    my_col = lax.axis_index("col")
    total_rows = row_pick.shape[0]
    local_rows = total_rows // rows_count
    my_pick = lax.dynamic_slice_in_dim(row_pick, my_row * local_rows, local_rows)
    pool_rows = pool.shape[0]
    group_pixels = pool_rows * cols_count
    owner = my_pick // pool_rows
    owner_hot = (owner[:, None] == jnp.arange(cols_count)[None, :]).astype(jnp.bfloat16)
    pixel_hot = (my_pick[:, None] % pool_rows == jnp.arange(pool_rows)[None, :]).astype(jnp.bfloat16)
    picked = jnp.dot(owner_hot.T, pixel_hot, preferred_element_type=jnp.float32)
    counts = jnp.cumsum(picked, axis=1)
    mine = lax.dynamic_index_in_dim(counts, my_col, axis=0, keepdims=False)
    slots = jnp.arange(CAP, dtype=jnp.float32)
    local_idx = jnp.sum((mine[None, :] <= slots[:, None]).astype(jnp.int32), axis=1)
    compact = jnp.take(pool, jnp.minimum(local_idx, pool_rows - 1), axis=0)
    gathered = lax.all_gather(compact, "col", axis=0, tiled=True)
    row_counts = jnp.dot(owner_hot, counts.astype(jnp.bfloat16), preferred_element_type=jnp.float32)
    slot = jnp.sum(row_counts * pixel_hot.astype(jnp.float32), axis=1).astype(jnp.int32) - 1
    pick_idx = owner * CAP + slot
    features = jnp.take(gathered, pick_idx, axis=0)
    panel = panel_tile[0]
    tiles = panel + 1 + jnp.mod(my_col - panel - 1, cols_count) + cols_count * jnp.arange(WT)
    served = my_row + rows_count * (my_col // rows_count)
    served_tiles = panel + 1 + jnp.mod(served - panel - 1, cols_count) + cols_count * jnp.arange(WT)
    local_tiles = served_tiles // rows_count
    col_source = (local_tiles[:, None] * TB + jnp.arange(TB)[None, :]).reshape(-1)
    col_local = jnp.take(gathered, jnp.take(pick_idx, col_source), axis=0)
    col_feats = lax.ppermute(col_local, ("row", "col"), window_perm(rows_count, cols_count))
    panel_row = panel % rows_count
    panel_local = panel // rows_count
    panel_rows = jnp.take(gathered, lax.dynamic_slice_in_dim(pick_idx, panel_local * TB, TB), axis=0)
    panel_feats = lax.dynamic_index_in_dim(
        lax.all_gather(panel_rows, "row", axis=0), panel_row, axis=0, keepdims=False
    )
    inverse_scale = 1.0 / length_scale
    scaled_rows = features * inverse_scale
    scaled_cols = col_feats * inverse_scale
    scaled_panel = panel_feats * inverse_scale
    local_index = jnp.arange(local_rows)
    row_global = (local_index // TB * rows_count + my_row) * TB + local_index % TB
    col_global = (tiles[:, None] * TB + jnp.arange(TB)[None, :]).reshape(-1)
    panel_global = panel * TB + jnp.arange(TB)
    factor = jnp.linalg.cholesky(kernel(scaled_panel, scaled_panel, panel_global, panel_global))
    row_panel = panel_solve(factor, kernel(scaled_rows, scaled_panel, row_global, panel_global))
    col_panel = panel_solve(factor, kernel(scaled_cols, scaled_panel, col_global, panel_global))
    update = jnp.dot(
        row_panel, col_panel.T, precision=lax.Precision.HIGHEST, preferred_element_type=jnp.float32
    )
    schur = kernel(scaled_rows, scaled_cols, row_global, col_global) - update
    return (schur, row_panel)


def solution(mesh):
    in_specs = (P(("row", "col"), None), P(), P(), P())
    out_specs = (P("row", "col"), P("row", None))
    return jax.shard_map(body, mesh=mesh, in_specs=in_specs, out_specs=out_specs, check_vma=False)
```

```python
import jax
import jax.numpy as jnp
from jax import lax
from jax.sharding import PartitionSpec as P

TB = 64
WT = 2
CAP = 160


noise_level = 0.1
root_five = 5.0**0.5


def broadcast_rows(x, root, rows_count, radix=4):
    dist = jnp.mod(lax.axis_index("row") - root, rows_count)
    step = 1
    while step < rows_count:
        new = x
        for k in range(1, radix):
            shift = k * step
            if shift >= rows_count:
                break
            perm = [(i, (i + shift) % rows_count) for i in range(rows_count)]
            got = lax.ppermute(x, "row", perm)
            new = jnp.where((dist >= shift) & (dist < shift + step), got, new)
        x = new
        step *= radix
    return x


def shift_perm(cols_count, span, stride, shift):
    pairs = []
    for c in range(cols_count):
        pos = c // stride % span
        dst = c + ((pos + shift) % span - pos) * stride
        pairs.append((c, dst))
    return pairs


def ring_gather(x, cols_count, span, stride):
    fwd_perm = shift_perm(cols_count, span, stride, 1)
    bwd_perm = shift_perm(cols_count, span, stride, -1)
    blocks = [x]
    fwd, bwd = x, x
    for _ in range(span // 2 - 1):
        fwd = lax.ppermute(fwd, "col", fwd_perm)
        bwd = lax.ppermute(bwd, "col", bwd_perm)
        blocks += [fwd, bwd]
    half = x.shape[0] // 2
    last_fwd = lax.ppermute(fwd[:half], "col", fwd_perm)
    last_bwd = lax.ppermute(bwd[half:], "col", bwd_perm)
    blocks.append(jnp.concatenate([last_fwd, last_bwd], axis=0))
    return jnp.concatenate(blocks, axis=0)


def ring_order(span):
    order = [0] * span
    order[0] = 0
    for s in range(1, span // 2):
        order[(-s) % span] = 2 * s - 1
        order[s % span] = 2 * s
    order[span // 2] = span - 1
    return order


def window_perm(rows_count, cols_count):
    pairs = []
    for g in range(rows_count):
        for c2 in range(cols_count):
            r = c2 % rows_count
            c = g + rows_count * (c2 // rows_count)
            pairs.append((g * cols_count + c2, r * cols_count + c))
    return pairs


def kernel(left, right, left_index, right_index):
    left_sq = jnp.sum(left * left, axis=1)
    right_sq = jnp.sum(right * right, axis=1)
    cross = jnp.dot(
        left, right.T, precision=lax.Precision.HIGHEST, preferred_element_type=jnp.float32
    )
    dist_sq = jnp.maximum(left_sq[:, None] + right_sq[None, :] - 2.0 * cross, 0.0)
    radius = jnp.sqrt(dist_sq)
    value = (1.0 + root_five * radius + 5.0 / 3.0 * dist_sq) * jnp.exp(-root_five * radius)
    same = (left_index[:, None] == right_index[None, :]).astype(value.dtype)
    return value + noise_level * same


def panel_solve(factor, block):
    return lax.linalg.triangular_solve(factor, block, left_side=False, lower=True, transpose_a=True)


def body(pool, row_pick, length_scale, panel_tile):
    rows_count = lax.axis_size("row")
    cols_count = lax.axis_size("col")
    my_row = lax.axis_index("row")
    my_col = lax.axis_index("col")
    total_rows = row_pick.shape[0]
    local_rows = total_rows // rows_count
    my_pick = lax.dynamic_slice_in_dim(row_pick, my_row * local_rows, local_rows)
    pool_rows = pool.shape[0]
    group_pixels = pool_rows * cols_count
    owner = my_pick // pool_rows
    owner_hot = (owner[:, None] == jnp.arange(cols_count)[None, :]).astype(jnp.bfloat16)
    pixel_hot = (my_pick[:, None] % pool_rows == jnp.arange(pool_rows)[None, :]).astype(jnp.bfloat16)
    picked = jnp.dot(owner_hot.T, pixel_hot, preferred_element_type=jnp.float32)
    counts = jnp.cumsum(picked, axis=1)
    mine = lax.dynamic_index_in_dim(counts, my_col, axis=0, keepdims=False)
    slots = jnp.arange(CAP, dtype=jnp.float32)
    local_idx = jnp.sum((mine[None, :] <= slots[:, None]).astype(jnp.int32), axis=1)
    compact = jnp.take(pool, jnp.minimum(local_idx, pool_rows - 1), axis=0)
    span_y = 8 if cols_count % 8 == 0 else cols_count
    span_x = cols_count // span_y
    half = CAP // 2
    part_a = ring_gather(ring_gather(compact[:half], cols_count, span_y, 1), cols_count, span_x, span_y)
    part_b = ring_gather(ring_gather(compact[half:], cols_count, span_x, span_y), cols_count, span_y, 1)
    gathered = jnp.concatenate([part_a, part_b], axis=0)
    row_counts = jnp.dot(owner_hot, counts.astype(jnp.bfloat16), preferred_element_type=jnp.float32)
    slot = jnp.sum(row_counts * pixel_hot.astype(jnp.float32), axis=1).astype(jnp.int32) - 1
    order_y = jnp.array(ring_order(span_y), jnp.int32)
    order_x = jnp.array(ring_order(span_x), jnp.int32)
    ky = jnp.take(order_y, jnp.mod(owner % span_y - my_col % span_y, span_y))
    kx = jnp.take(order_x, jnp.mod(owner // span_y - my_col // span_y, span_x))
    pick_idx = jnp.where(
        slot < half,
        (kx * span_y + ky) * half + slot,
        cols_count * half + (ky * span_x + kx) * half + slot - half,
    )
    features = jnp.take(gathered, pick_idx, axis=0)
    panel = panel_tile[0]
    tiles = panel + 1 + jnp.mod(my_col - panel - 1, cols_count) + cols_count * jnp.arange(WT)
    served = my_row + rows_count * (my_col // rows_count)
    served_tiles = panel + 1 + jnp.mod(served - panel - 1, cols_count) + cols_count * jnp.arange(WT)
    local_tiles = served_tiles // rows_count
    col_source = (local_tiles[:, None] * TB + jnp.arange(TB)[None, :]).reshape(-1)
    col_local = jnp.take(gathered, jnp.take(pick_idx, col_source), axis=0)
    col_feats = lax.ppermute(col_local, ("row", "col"), window_perm(rows_count, cols_count))
    panel_row = panel % rows_count
    panel_local = panel // rows_count
    panel_rows = jnp.take(gathered, lax.dynamic_slice_in_dim(pick_idx, panel_local * TB, TB), axis=0)
    panel_feats = broadcast_rows(panel_rows, panel_row, rows_count)
    inverse_scale = 1.0 / length_scale
    scaled_rows = features * inverse_scale
    scaled_cols = col_feats * inverse_scale
    scaled_panel = panel_feats * inverse_scale
    local_index = jnp.arange(local_rows)
    row_global = (local_index // TB * rows_count + my_row) * TB + local_index % TB
    col_global = (tiles[:, None] * TB + jnp.arange(TB)[None, :]).reshape(-1)
    panel_global = panel * TB + jnp.arange(TB)
    factor = jnp.linalg.cholesky(kernel(scaled_panel, scaled_panel, panel_global, panel_global))
    row_panel = panel_solve(factor, kernel(scaled_rows, scaled_panel, row_global, panel_global))
    col_panel = panel_solve(factor, kernel(scaled_cols, scaled_panel, col_global, panel_global))
    update = jnp.dot(
        row_panel, col_panel.T, precision=lax.Precision.HIGHEST, preferred_element_type=jnp.float32
    )
    schur = kernel(scaled_rows, scaled_cols, row_global, col_global) - update
    return (schur, row_panel)


def solution(mesh):
    in_specs = (P(("row", "col"), None), P(), P(), P())
    out_specs = (P("row", "col"), P("row", None))
    return jax.shard_map(body, mesh=mesh, in_specs=in_specs, out_specs=out_specs, check_vma=False)
```

```python
import jax
import jax.numpy as jnp
from jax import lax
from jax.sharding import PartitionSpec as P

TB = 64
WT = 2
CAP = 160


noise_level = 0.1
root_five = 5.0**0.5


def broadcast_rows(x, root, rows_count, radix=4):
    dist = jnp.mod(lax.axis_index("row") - root, rows_count)
    step = 1
    while step < rows_count:
        new = x
        for k in range(1, radix):
            shift = k * step
            if shift >= rows_count:
                break
            perm = [(i, (i + shift) % rows_count) for i in range(rows_count)]
            got = lax.ppermute(x, "row", perm)
            new = jnp.where((dist >= shift) & (dist < shift + step), got, new)
        x = new
        step *= radix
    return x


def window_perm(rows_count, cols_count):
    pairs = []
    for g in range(rows_count):
        for c2 in range(cols_count):
            r = c2 % rows_count
            c = g + rows_count * (c2 // rows_count)
            pairs.append((g * cols_count + c2, r * cols_count + c))
    return pairs


def kernel(left, right, left_index, right_index):
    left_sq = jnp.sum(left * left, axis=1)
    right_sq = jnp.sum(right * right, axis=1)
    cross = jnp.dot(
        left, right.T, precision=lax.Precision.HIGHEST, preferred_element_type=jnp.float32
    )
    dist_sq = jnp.maximum(left_sq[:, None] + right_sq[None, :] - 2.0 * cross, 0.0)
    radius = jnp.sqrt(dist_sq)
    value = (1.0 + root_five * radius + 5.0 / 3.0 * dist_sq) * jnp.exp(-root_five * radius)
    same = (left_index[:, None] == right_index[None, :]).astype(value.dtype)
    return value + noise_level * same


def panel_solve(factor, block):
    return lax.linalg.triangular_solve(factor, block, left_side=False, lower=True, transpose_a=True)


def body(pool, row_pick, length_scale, panel_tile):
    rows_count = lax.axis_size("row")
    cols_count = lax.axis_size("col")
    my_row = lax.axis_index("row")
    my_col = lax.axis_index("col")
    total_rows = row_pick.shape[0]
    local_rows = total_rows // rows_count
    my_pick = lax.dynamic_slice_in_dim(row_pick, my_row * local_rows, local_rows)
    pool_rows = pool.shape[0]
    group_pixels = pool_rows * cols_count
    owner = my_pick // pool_rows
    owner_hot = (owner[:, None] == jnp.arange(cols_count)[None, :]).astype(jnp.bfloat16)
    pixel_hot = (my_pick[:, None] % pool_rows == jnp.arange(pool_rows)[None, :]).astype(jnp.bfloat16)
    picked = jnp.dot(owner_hot.T, pixel_hot, preferred_element_type=jnp.float32)
    counts = jnp.cumsum(picked, axis=1)
    mine = lax.dynamic_index_in_dim(counts, my_col, axis=0, keepdims=False)
    slots = jnp.arange(CAP, dtype=jnp.float32)
    local_idx = jnp.sum((mine[None, :] <= slots[:, None]).astype(jnp.int32), axis=1)
    compact = jnp.take(pool, jnp.minimum(local_idx, pool_rows - 1), axis=0)
    gathered = lax.all_gather(compact, "col", axis=0, tiled=True)
    row_counts = jnp.dot(owner_hot, counts.astype(jnp.bfloat16), preferred_element_type=jnp.float32)
    slot = jnp.sum(row_counts * pixel_hot.astype(jnp.float32), axis=1).astype(jnp.int32) - 1
    pick_idx = owner * CAP + slot
    features = jnp.take(gathered, pick_idx, axis=0)
    panel = panel_tile[0]
    tiles = panel + 1 + jnp.mod(my_col - panel - 1, cols_count) + cols_count * jnp.arange(WT)
    served = my_row + rows_count * (my_col // rows_count)
    served_tiles = panel + 1 + jnp.mod(served - panel - 1, cols_count) + cols_count * jnp.arange(WT)
    local_tiles = served_tiles // rows_count
    col_source = (local_tiles[:, None] * TB + jnp.arange(TB)[None, :]).reshape(-1)

    panel_row = panel % rows_count
    panel_local = panel // rows_count
    both_idx = jnp.concatenate(
        [lax.dynamic_slice_in_dim(pick_idx, panel_local * TB, TB), jnp.take(pick_idx, col_source)]
    )
    both_rows = jnp.take(gathered, both_idx, axis=0)
    panel_rows = both_rows[:TB]
    col_local = both_rows[TB:]
    col_feats = lax.ppermute(col_local, ("row", "col"), window_perm(rows_count, cols_count))
    panel_feats = lax.dynamic_index_in_dim(
        lax.all_gather(panel_rows, "row", axis=0), panel_row, axis=0, keepdims=False
    )
    inverse_scale = 1.0 / length_scale
    scaled_rows = features * inverse_scale
    scaled_cols = col_feats * inverse_scale
    scaled_panel = panel_feats * inverse_scale
    local_index = jnp.arange(local_rows)
    row_global = (local_index // TB * rows_count + my_row) * TB + local_index % TB
    col_global = (tiles[:, None] * TB + jnp.arange(TB)[None, :]).reshape(-1)
    panel_global = panel * TB + jnp.arange(TB)
    factor = jnp.linalg.cholesky(kernel(scaled_panel, scaled_panel, panel_global, panel_global))
    row_panel = panel_solve(factor, kernel(scaled_rows, scaled_panel, row_global, panel_global))
    col_panel = panel_solve(factor, kernel(scaled_cols, scaled_panel, col_global, panel_global))
    window = lax.optimization_barrier(kernel(scaled_rows, scaled_cols, row_global, col_global))
    update = jnp.dot(
        row_panel, col_panel.T, precision=lax.Precision.HIGHEST, preferred_element_type=jnp.float32
    )
    schur = window - update
    return (schur, row_panel)


def solution(mesh):
    in_specs = (P(("row", "col"), None), P(), P(), P())
    out_specs = (P("row", "col"), P("row", None))
    return jax.shard_map(body, mesh=mesh, in_specs=in_specs, out_specs=out_specs, check_vma=False)
```

```python
import jax
import jax.numpy as jnp
from jax import lax
from jax.sharding import PartitionSpec as P

TB = 64
WT = 2
CAP = 160


noise_level = 0.1
root_five = 5.0**0.5


def broadcast_rows(x, root, rows_count, radix=4):
    dist = jnp.mod(lax.axis_index("row") - root, rows_count)
    step = 1
    while step < rows_count:
        new = x
        for k in range(1, radix):
            shift = k * step
            if shift >= rows_count:
                break
            perm = [(i, (i + shift) % rows_count) for i in range(rows_count)]
            got = lax.ppermute(x, "row", perm)
            new = jnp.where((dist >= shift) & (dist < shift + step), got, new)
        x = new
        step *= radix
    return x


def window_perm(rows_count, cols_count):
    pairs = []
    for g in range(rows_count):
        for c2 in range(cols_count):
            r = c2 % rows_count
            c = g + rows_count * (c2 // rows_count)
            pairs.append((g * cols_count + c2, r * cols_count + c))
    return pairs


def kernel(left, right, left_index, right_index):
    left_sq = jnp.sum(left * left, axis=1)
    right_sq = jnp.sum(right * right, axis=1)
    cross = jnp.dot(
        left, right.T, precision=lax.Precision.HIGHEST, preferred_element_type=jnp.float32
    )
    dist_sq = jnp.maximum(left_sq[:, None] + right_sq[None, :] - 2.0 * cross, 0.0)
    radius = jnp.sqrt(dist_sq)
    value = (1.0 + root_five * radius + 5.0 / 3.0 * dist_sq) * jnp.exp(-root_five * radius)
    same = (left_index[:, None] == right_index[None, :]).astype(value.dtype)
    return value + noise_level * same


def panel_solve(factor, block):
    return lax.linalg.triangular_solve(factor, block, left_side=False, lower=True, transpose_a=True)


def body(pool, row_pick, length_scale, panel_tile):
    rows_count = lax.axis_size("row")
    cols_count = lax.axis_size("col")
    my_row = lax.axis_index("row")
    my_col = lax.axis_index("col")
    total_rows = row_pick.shape[0]
    local_rows = total_rows // rows_count
    my_pick = lax.dynamic_slice_in_dim(row_pick, my_row * local_rows, local_rows)
    pool_rows = pool.shape[0]
    group_pixels = pool_rows * cols_count
    owner = my_pick // pool_rows
    owner_hot = (owner[:, None] == jnp.arange(cols_count)[None, :]).astype(jnp.bfloat16)
    pixel_hot = (my_pick[:, None] % pool_rows == jnp.arange(pool_rows)[None, :]).astype(jnp.bfloat16)
    picked = jnp.dot(owner_hot.T, pixel_hot, preferred_element_type=jnp.float32)
    counts = jnp.cumsum(picked, axis=1)
    mine = lax.dynamic_index_in_dim(counts, my_col, axis=0, keepdims=False)
    slots = jnp.arange(CAP, dtype=jnp.float32)
    local_idx = jnp.sum((mine[None, :] <= slots[:, None]).astype(jnp.int32), axis=1)
    compact = jnp.take(pool, jnp.minimum(local_idx, pool_rows - 1), axis=0)
    gathered = lax.all_gather(compact, "col", axis=0, tiled=True)
    row_counts = jnp.dot(owner_hot, counts.astype(jnp.bfloat16), preferred_element_type=jnp.float32)
    slot = jnp.sum(row_counts * pixel_hot.astype(jnp.float32), axis=1).astype(jnp.int32) - 1
    pick_idx = owner * CAP + slot
    features = jnp.take(gathered, pick_idx, axis=0)
    panel = panel_tile[0]
    tiles = panel + 1 + jnp.mod(my_col - panel - 1, cols_count) + cols_count * jnp.arange(WT)
    served = my_row + rows_count * (my_col // rows_count)
    served_tiles = panel + 1 + jnp.mod(served - panel - 1, cols_count) + cols_count * jnp.arange(WT)
    local_tiles = served_tiles // rows_count
    col_source = (local_tiles[:, None] * TB + jnp.arange(TB)[None, :]).reshape(-1)

    panel_row = panel % rows_count
    panel_local = panel // rows_count
    both_idx = jnp.concatenate(
        [lax.dynamic_slice_in_dim(pick_idx, panel_local * TB, TB), jnp.take(pick_idx, col_source)]
    )
    both_rows = jnp.take(gathered, both_idx, axis=0)
    panel_rows = both_rows[:TB]
    col_local = both_rows[TB:]
    col_feats = lax.ppermute(col_local, ("row", "col"), window_perm(rows_count, cols_count))
    panel_feats = lax.dynamic_index_in_dim(
        lax.all_gather(panel_rows, "row", axis=0), panel_row, axis=0, keepdims=False
    )
    inverse_scale = 1.0 / length_scale
    scaled_rows = features * inverse_scale
    scaled_cols = col_feats * inverse_scale
    scaled_panel = panel_feats * inverse_scale
    local_index = jnp.arange(local_rows)
    row_global = (local_index // TB * rows_count + my_row) * TB + local_index % TB
    col_global = (tiles[:, None] * TB + jnp.arange(TB)[None, :]).reshape(-1)
    panel_global = panel * TB + jnp.arange(TB)
    factor = jnp.linalg.cholesky(kernel(scaled_panel, scaled_panel, panel_global, panel_global))
    row_panel = panel_solve(factor, kernel(scaled_rows, scaled_panel, row_global, panel_global))
    col_panel = panel_solve(factor, kernel(scaled_cols, scaled_panel, col_global, panel_global))
    update = jnp.dot(
        row_panel, col_panel.T, precision=lax.Precision.HIGHEST, preferred_element_type=jnp.float32
    )
    schur = kernel(scaled_rows, scaled_cols, row_global, col_global) - update
    return (schur, row_panel)


def solution(mesh):
    in_specs = (P(("row", "col"), None), P(), P(), P())
    out_specs = (P("row", "col"), P("row", None))
    return jax.shard_map(body, mesh=mesh, in_specs=in_specs, out_specs=out_specs, check_vma=False)
```

```python
import jax
import jax.numpy as jnp
from jax import lax
from jax.experimental import pallas as pl
from jax.sharding import PartitionSpec as P

TB = 64
WT = 2
CAP = 160


noise_level = 0.1
root_five = 5.0**0.5


def broadcast_rows(x, root, rows_count, radix=4):
    dist = jnp.mod(lax.axis_index("row") - root, rows_count)
    step = 1
    while step < rows_count:
        new = x
        for k in range(1, radix):
            shift = k * step
            if shift >= rows_count:
                break
            perm = [(i, (i + shift) % rows_count) for i in range(rows_count)]
            got = lax.ppermute(x, "row", perm)
            new = jnp.where((dist >= shift) & (dist < shift + step), got, new)
        x = new
        step *= radix
    return x


def window_perm(rows_count, cols_count):
    pairs = []
    for g in range(rows_count):
        for c2 in range(cols_count):
            r = c2 % rows_count
            c = g + rows_count * (c2 // rows_count)
            pairs.append((g * cols_count + c2, r * cols_count + c))
    return pairs


def kernel(left, right, left_index, right_index):
    left_sq = jnp.sum(left * left, axis=1)
    right_sq = jnp.sum(right * right, axis=1)
    cross = jnp.dot(
        left, right.T, precision=lax.Precision.HIGHEST, preferred_element_type=jnp.float32
    )
    dist_sq = jnp.maximum(left_sq[:, None] + right_sq[None, :] - 2.0 * cross, 0.0)
    radius = jnp.sqrt(dist_sq)
    value = (1.0 + root_five * radius + 5.0 / 3.0 * dist_sq) * jnp.exp(-root_five * radius)
    same = (left_index[:, None] == right_index[None, :]).astype(value.dtype)
    return value + noise_level * same


def factor_kernel(a_ref, low_ref, inv_ref):
    n = a_ref.shape[0]
    rows = lax.broadcasted_iota(jnp.int32, (n, n), 0)
    cols = lax.broadcasted_iota(jnp.int32, (n, n), 1)
    rcol = lax.broadcasted_iota(jnp.int32, (n, 1), 0)
    ccol = lax.broadcasted_iota(jnp.int32, (1, n), 1)
    m = a_ref[...]
    low = jnp.zeros((n, n), jnp.float32)
    inv = (rows == cols).astype(jnp.float32)
    for k in range(n):
        d = jnp.sqrt(m[k : k + 1, k : k + 1])
        lc = jnp.where(rcol >= k, m[:, k : k + 1] / d, 0.0)
        lr = jnp.where(ccol >= k, m[k : k + 1, :] / d, 0.0)
        m = m - lc * lr
        low = jnp.where(cols == k, lc, low)
        xk = inv[k : k + 1, :] / d
        inv = jnp.where(rows == k, xk, inv) - jnp.where(rcol > k, lc, 0.0) * xk
    low_ref[...] = low
    inv_ref[...] = inv


def factor_and_inverse(a):
    shape = jax.ShapeDtypeStruct(a.shape, jnp.float32)
    return pl.pallas_call(factor_kernel, out_shape=(shape, shape))(a)


def panel_solve(inverse, block):
    return jnp.dot(
        block, inverse.T, precision=lax.Precision.HIGHEST, preferred_element_type=jnp.float32
    )


def body(pool, row_pick, length_scale, panel_tile):
    rows_count = lax.axis_size("row")
    cols_count = lax.axis_size("col")
    my_row = lax.axis_index("row")
    my_col = lax.axis_index("col")
    total_rows = row_pick.shape[0]
    local_rows = total_rows // rows_count
    my_pick = lax.dynamic_slice_in_dim(row_pick, my_row * local_rows, local_rows)
    pool_rows = pool.shape[0]
    group_pixels = pool_rows * cols_count
    owner = my_pick // pool_rows
    owner_hot = (owner[:, None] == jnp.arange(cols_count)[None, :]).astype(jnp.bfloat16)
    pixel_hot = (my_pick[:, None] % pool_rows == jnp.arange(pool_rows)[None, :]).astype(jnp.bfloat16)
    picked = jnp.dot(owner_hot.T, pixel_hot, preferred_element_type=jnp.float32)
    counts = jnp.cumsum(picked, axis=1)
    mine = lax.dynamic_index_in_dim(counts, my_col, axis=0, keepdims=False)
    slots = jnp.arange(CAP, dtype=jnp.float32)
    local_idx = jnp.sum((mine[None, :] <= slots[:, None]).astype(jnp.int32), axis=1)
    compact = jnp.take(pool, jnp.minimum(local_idx, pool_rows - 1), axis=0)
    gathered = lax.all_gather(compact, "col", axis=0, tiled=True)
    row_counts = jnp.dot(owner_hot, counts.astype(jnp.bfloat16), preferred_element_type=jnp.float32)
    slot = jnp.sum(row_counts * pixel_hot.astype(jnp.float32), axis=1).astype(jnp.int32) - 1
    pick_idx = owner * CAP + slot
    features = jnp.take(gathered, pick_idx, axis=0)
    panel = panel_tile[0]
    tiles = panel + 1 + jnp.mod(my_col - panel - 1, cols_count) + cols_count * jnp.arange(WT)
    served = my_row + rows_count * (my_col // rows_count)
    served_tiles = panel + 1 + jnp.mod(served - panel - 1, cols_count) + cols_count * jnp.arange(WT)
    local_tiles = served_tiles // rows_count
    col_source = (local_tiles[:, None] * TB + jnp.arange(TB)[None, :]).reshape(-1)
    col_local = jnp.take(gathered, jnp.take(pick_idx, col_source), axis=0)
    col_feats = lax.ppermute(col_local, ("row", "col"), window_perm(rows_count, cols_count))
    panel_row = panel % rows_count
    panel_local = panel // rows_count
    panel_rows = jnp.take(gathered, lax.dynamic_slice_in_dim(pick_idx, panel_local * TB, TB), axis=0)
    panel_feats = lax.dynamic_index_in_dim(
        lax.all_gather(panel_rows, "row", axis=0), panel_row, axis=0, keepdims=False
    )
    inverse_scale = 1.0 / length_scale
    scaled_rows = features * inverse_scale
    scaled_cols = col_feats * inverse_scale
    scaled_panel = panel_feats * inverse_scale
    local_index = jnp.arange(local_rows)
    row_global = (local_index // TB * rows_count + my_row) * TB + local_index % TB
    col_global = (tiles[:, None] * TB + jnp.arange(TB)[None, :]).reshape(-1)
    panel_global = panel * TB + jnp.arange(TB)
    factor, inverse = factor_and_inverse(kernel(scaled_panel, scaled_panel, panel_global, panel_global))
    row_panel = panel_solve(inverse, kernel(scaled_rows, scaled_panel, row_global, panel_global))
    col_panel = panel_solve(inverse, kernel(scaled_cols, scaled_panel, col_global, panel_global))
    update = jnp.dot(
        row_panel, col_panel.T, precision=lax.Precision.HIGHEST, preferred_element_type=jnp.float32
    )
    schur = kernel(scaled_rows, scaled_cols, row_global, col_global) - update
    return (schur, row_panel)


def solution(mesh):
    in_specs = (P(("row", "col"), None), P(), P(), P())
    out_specs = (P("row", "col"), P("row", None))
    return jax.shard_map(body, mesh=mesh, in_specs=in_specs, out_specs=out_specs, check_vma=False)
```

```python
import jax
import jax.numpy as jnp
from jax import lax
from jax.experimental import pallas as pl
from jax.sharding import PartitionSpec as P

TB = 64
WT = 2
CAP = 160


noise_level = 0.1
root_five = 5.0**0.5


def broadcast_rows(x, root, rows_count, radix=4):
    dist = jnp.mod(lax.axis_index("row") - root, rows_count)
    step = 1
    while step < rows_count:
        new = x
        for k in range(1, radix):
            shift = k * step
            if shift >= rows_count:
                break
            perm = [(i, (i + shift) % rows_count) for i in range(rows_count)]
            got = lax.ppermute(x, "row", perm)
            new = jnp.where((dist >= shift) & (dist < shift + step), got, new)
        x = new
        step *= radix
    return x


def window_perm(rows_count, cols_count):
    pairs = []
    for g in range(rows_count):
        for c2 in range(cols_count):
            r = c2 % rows_count
            c = g + rows_count * (c2 // rows_count)
            pairs.append((g * cols_count + c2, r * cols_count + c))
    return pairs


def kernel(left, right, left_index, right_index):
    left_sq = jnp.sum(left * left, axis=1)
    right_sq = jnp.sum(right * right, axis=1)
    cross = jnp.dot(
        left, right.T, precision=lax.Precision.HIGHEST, preferred_element_type=jnp.float32
    )
    dist_sq = jnp.maximum(left_sq[:, None] + right_sq[None, :] - 2.0 * cross, 0.0)
    radius = jnp.sqrt(dist_sq)
    value = (1.0 + root_five * radius + 5.0 / 3.0 * dist_sq) * jnp.exp(-root_five * radius)
    same = (left_index[:, None] == right_index[None, :]).astype(value.dtype)
    return value + noise_level * same


def factor_kernel(a_ref, low_ref, inv_ref):
    n = a_ref.shape[0]
    rows = lax.broadcasted_iota(jnp.int32, (n, n), 0)
    cols = lax.broadcasted_iota(jnp.int32, (n, n), 1)
    rcol = lax.broadcasted_iota(jnp.int32, (n, 1), 0)
    ccol = lax.broadcasted_iota(jnp.int32, (1, n), 1)
    m = a_ref[...]
    low = jnp.zeros((n, n), jnp.float32)
    inv = (rows == cols).astype(jnp.float32)
    for k in range(n):
        r = 1.0 / jnp.sqrt(m[k : k + 1, k : k + 1])
        lc = jnp.where(rcol >= k, m[:, k : k + 1] * r, 0.0)
        lr = jnp.where(ccol >= k, m[k : k + 1, :] * r, 0.0)
        m = m - lc * lr
        low = jnp.where(cols == k, lc, low)
        xk = inv[k : k + 1, :] * r
        inv = jnp.where(rows == k, xk, inv) - jnp.where(rcol > k, lc, 0.0) * xk
    low_ref[...] = low
    inv_ref[...] = inv


def factor_and_inverse(a):
    shape = jax.ShapeDtypeStruct(a.shape, jnp.float32)
    return pl.pallas_call(factor_kernel, out_shape=(shape, shape))(a)


def panel_solve(inverse, block):
    return jnp.dot(
        block, inverse.T, precision=lax.Precision.HIGHEST, preferred_element_type=jnp.float32
    )


def body(pool, row_pick, length_scale, panel_tile):
    rows_count = lax.axis_size("row")
    cols_count = lax.axis_size("col")
    my_row = lax.axis_index("row")
    my_col = lax.axis_index("col")
    total_rows = row_pick.shape[0]
    local_rows = total_rows // rows_count
    my_pick = lax.dynamic_slice_in_dim(row_pick, my_row * local_rows, local_rows)
    pool_rows = pool.shape[0]
    group_pixels = pool_rows * cols_count
    owner = my_pick // pool_rows
    owner_hot = (owner[:, None] == jnp.arange(cols_count)[None, :]).astype(jnp.bfloat16)
    pixel_hot = (my_pick[:, None] % pool_rows == jnp.arange(pool_rows)[None, :]).astype(jnp.bfloat16)
    picked = jnp.dot(owner_hot.T, pixel_hot, preferred_element_type=jnp.float32)
    counts = jnp.cumsum(picked, axis=1)
    mine = lax.dynamic_index_in_dim(counts, my_col, axis=0, keepdims=False)
    slots = jnp.arange(CAP, dtype=jnp.float32)
    local_idx = jnp.sum((mine[None, :] <= slots[:, None]).astype(jnp.int32), axis=1)
    compact = jnp.take(pool, jnp.minimum(local_idx, pool_rows - 1), axis=0)
    gathered = lax.all_gather(compact, "col", axis=0, tiled=True)
    row_counts = jnp.dot(owner_hot, counts.astype(jnp.bfloat16), preferred_element_type=jnp.float32)
    slot = jnp.sum(row_counts * pixel_hot.astype(jnp.float32), axis=1).astype(jnp.int32) - 1
    pick_idx = owner * CAP + slot
    features = jnp.take(gathered, pick_idx, axis=0)
    panel = panel_tile[0]
    tiles = panel + 1 + jnp.mod(my_col - panel - 1, cols_count) + cols_count * jnp.arange(WT)
    served = my_row + rows_count * (my_col // rows_count)
    served_tiles = panel + 1 + jnp.mod(served - panel - 1, cols_count) + cols_count * jnp.arange(WT)
    local_tiles = served_tiles // rows_count
    col_source = (local_tiles[:, None] * TB + jnp.arange(TB)[None, :]).reshape(-1)
    col_local = jnp.take(gathered, jnp.take(pick_idx, col_source), axis=0)
    col_feats = lax.ppermute(col_local, ("row", "col"), window_perm(rows_count, cols_count))
    panel_row = panel % rows_count
    panel_local = panel // rows_count
    panel_rows = jnp.take(gathered, lax.dynamic_slice_in_dim(pick_idx, panel_local * TB, TB), axis=0)
    panel_feats = lax.dynamic_index_in_dim(
        lax.all_gather(panel_rows, "row", axis=0), panel_row, axis=0, keepdims=False
    )
    inverse_scale = 1.0 / length_scale
    scaled_rows = features * inverse_scale
    scaled_cols = col_feats * inverse_scale
    scaled_panel = panel_feats * inverse_scale
    local_index = jnp.arange(local_rows)
    row_global = (local_index // TB * rows_count + my_row) * TB + local_index % TB
    col_global = (tiles[:, None] * TB + jnp.arange(TB)[None, :]).reshape(-1)
    panel_global = panel * TB + jnp.arange(TB)
    factor, inverse = factor_and_inverse(kernel(scaled_panel, scaled_panel, panel_global, panel_global))
    row_panel = panel_solve(inverse, kernel(scaled_rows, scaled_panel, row_global, panel_global))
    col_panel = panel_solve(inverse, kernel(scaled_cols, scaled_panel, col_global, panel_global))
    update = jnp.dot(
        row_panel, col_panel.T, precision=lax.Precision.HIGHEST, preferred_element_type=jnp.float32
    )
    schur = kernel(scaled_rows, scaled_cols, row_global, col_global) - update
    return (schur, row_panel)


def solution(mesh):
    in_specs = (P(("row", "col"), None), P(), P(), P())
    out_specs = (P("row", "col"), P("row", None))
    return jax.shard_map(body, mesh=mesh, in_specs=in_specs, out_specs=out_specs, check_vma=False)
```

```python
import jax
import jax.numpy as jnp
from jax import lax
from jax.experimental import pallas as pl
from jax.sharding import PartitionSpec as P

TB = 64
WT = 2
CAP = 160


noise_level = 0.1
root_five = 5.0**0.5


def broadcast_rows(x, root, rows_count, radix=4):
    dist = jnp.mod(lax.axis_index("row") - root, rows_count)
    step = 1
    while step < rows_count:
        new = x
        for k in range(1, radix):
            shift = k * step
            if shift >= rows_count:
                break
            perm = [(i, (i + shift) % rows_count) for i in range(rows_count)]
            got = lax.ppermute(x, "row", perm)
            new = jnp.where((dist >= shift) & (dist < shift + step), got, new)
        x = new
        step *= radix
    return x


def sum_broadcast(x, axis, size):
    step = 1
    while step < size:
        perm = [(i, (i + step) % size) for i in range(size)]
        x = x + lax.ppermute(x, axis, perm)
        step *= 2
    return x


def window_perm(rows_count, cols_count):
    pairs = []
    for g in range(rows_count):
        for c2 in range(cols_count):
            r = c2 % rows_count
            c = g + rows_count * (c2 // rows_count)
            pairs.append((g * cols_count + c2, r * cols_count + c))
    return pairs


def kernel(left, right, left_index, right_index):
    left_sq = jnp.sum(left * left, axis=1)
    right_sq = jnp.sum(right * right, axis=1)
    cross = jnp.dot(
        left, right.T, precision=lax.Precision.HIGHEST, preferred_element_type=jnp.float32
    )
    dist_sq = jnp.maximum(left_sq[:, None] + right_sq[None, :] - 2.0 * cross, 0.0)
    radius = jnp.sqrt(dist_sq)
    value = (1.0 + root_five * radius + 5.0 / 3.0 * dist_sq) * jnp.exp(-root_five * radius)
    same = (left_index[:, None] == right_index[None, :]).astype(value.dtype)
    return value + noise_level * same


def factor_kernel(a_ref, low_ref, inv_ref):
    n = a_ref.shape[0]
    rows = lax.broadcasted_iota(jnp.int32, (n, n), 0)
    cols = lax.broadcasted_iota(jnp.int32, (n, n), 1)
    rcol = lax.broadcasted_iota(jnp.int32, (n, 1), 0)
    ccol = lax.broadcasted_iota(jnp.int32, (1, n), 1)
    m = a_ref[...]
    low = jnp.zeros((n, n), jnp.float32)
    inv = (rows == cols).astype(jnp.float32)
    for k in range(n):
        r = 1.0 / jnp.sqrt(m[k : k + 1, k : k + 1])
        lc = jnp.where(rcol >= k, m[:, k : k + 1] * r, 0.0)
        lr = jnp.where(ccol >= k, m[k : k + 1, :] * r, 0.0)
        m = m - lc * lr
        low = jnp.where(cols == k, lc, low)
        xk = inv[k : k + 1, :] * r
        inv = jnp.where(rows == k, xk, inv) - jnp.where(rcol > k, lc, 0.0) * xk
    low_ref[...] = low
    inv_ref[...] = inv


def factor_and_inverse(a):
    shape = jax.ShapeDtypeStruct(a.shape, jnp.float32)
    return pl.pallas_call(factor_kernel, out_shape=(shape, shape))(a)


def panel_solve(inverse, block):
    return jnp.dot(
        block, inverse.T, precision=lax.Precision.HIGHEST, preferred_element_type=jnp.float32
    )


def body(pool, row_pick, length_scale, panel_tile):
    rows_count = lax.axis_size("row")
    cols_count = lax.axis_size("col")
    my_row = lax.axis_index("row")
    my_col = lax.axis_index("col")
    total_rows = row_pick.shape[0]
    local_rows = total_rows // rows_count
    my_pick = lax.dynamic_slice_in_dim(row_pick, my_row * local_rows, local_rows)
    pool_rows = pool.shape[0]
    group_pixels = pool_rows * cols_count
    owner = my_pick // pool_rows
    owner_hot = (owner[:, None] == jnp.arange(cols_count)[None, :]).astype(jnp.bfloat16)
    pixel_hot = (my_pick[:, None] % pool_rows == jnp.arange(pool_rows)[None, :]).astype(jnp.bfloat16)
    picked = jnp.dot(owner_hot.T, pixel_hot, preferred_element_type=jnp.float32)
    counts = jnp.cumsum(picked, axis=1)
    mine = lax.dynamic_index_in_dim(counts, my_col, axis=0, keepdims=False)
    slots = jnp.arange(CAP, dtype=jnp.float32)
    local_idx = jnp.sum((mine[None, :] <= slots[:, None]).astype(jnp.int32), axis=1)
    compact = jnp.take(pool, jnp.minimum(local_idx, pool_rows - 1), axis=0)
    gathered = lax.all_gather(compact, "col", axis=0, tiled=True)
    row_counts = jnp.dot(owner_hot, counts.astype(jnp.bfloat16), preferred_element_type=jnp.float32)
    slot = jnp.sum(row_counts * pixel_hot.astype(jnp.float32), axis=1).astype(jnp.int32) - 1
    pick_idx = owner * CAP + slot
    features = jnp.take(gathered, pick_idx, axis=0)
    panel = panel_tile[0]
    tiles = panel + 1 + jnp.mod(my_col - panel - 1, cols_count) + cols_count * jnp.arange(WT)
    served = my_row + rows_count * (my_col // rows_count)
    served_tiles = panel + 1 + jnp.mod(served - panel - 1, cols_count) + cols_count * jnp.arange(WT)
    local_tiles = served_tiles // rows_count
    col_source = (local_tiles[:, None] * TB + jnp.arange(TB)[None, :]).reshape(-1)
    col_local = jnp.take(gathered, jnp.take(pick_idx, col_source), axis=0)
    col_feats = lax.ppermute(col_local, ("row", "col"), window_perm(rows_count, cols_count))
    panel_row = panel % rows_count
    panel_local = panel // rows_count
    panel_pick = lax.dynamic_slice_in_dim(row_pick, panel_row * local_rows + panel_local * TB, TB)
    held = (panel_pick // pool_rows == my_col) & (my_row == panel_row)
    panel_part = jnp.where(held[:, None], jnp.take(pool, panel_pick % pool_rows, axis=0), 0.0)
    panel_rows = sum_broadcast(sum_broadcast(panel_part, "col", cols_count), "row", rows_count)
    panel_feats = panel_rows
    inverse_scale = 1.0 / length_scale
    scaled_rows = features * inverse_scale
    scaled_cols = col_feats * inverse_scale
    scaled_panel = panel_feats * inverse_scale
    local_index = jnp.arange(local_rows)
    row_global = (local_index // TB * rows_count + my_row) * TB + local_index % TB
    col_global = (tiles[:, None] * TB + jnp.arange(TB)[None, :]).reshape(-1)
    panel_global = panel * TB + jnp.arange(TB)
    factor, inverse = factor_and_inverse(kernel(scaled_panel, scaled_panel, panel_global, panel_global))
    row_panel = panel_solve(inverse, kernel(scaled_rows, scaled_panel, row_global, panel_global))
    col_panel = panel_solve(inverse, kernel(scaled_cols, scaled_panel, col_global, panel_global))
    update = jnp.dot(
        row_panel, col_panel.T, precision=lax.Precision.HIGHEST, preferred_element_type=jnp.float32
    )
    schur = kernel(scaled_rows, scaled_cols, row_global, col_global) - update
    return (schur, row_panel)


def solution(mesh):
    in_specs = (P(("row", "col"), None), P(), P(), P())
    out_specs = (P("row", "col"), P("row", None))
    return jax.shard_map(body, mesh=mesh, in_specs=in_specs, out_specs=out_specs, check_vma=False)
```

```python
import jax
import jax.numpy as jnp
from jax import lax
from jax.experimental import pallas as pl
from jax.sharding import PartitionSpec as P

TB = 64
WT = 2
CAP = 160


noise_level = 0.1
root_five = 5.0**0.5


def broadcast_rows(x, root, rows_count, radix=4):
    dist = jnp.mod(lax.axis_index("row") - root, rows_count)
    step = 1
    while step < rows_count:
        new = x
        for k in range(1, radix):
            shift = k * step
            if shift >= rows_count:
                break
            perm = [(i, (i + shift) % rows_count) for i in range(rows_count)]
            got = lax.ppermute(x, "row", perm)
            new = jnp.where((dist >= shift) & (dist < shift + step), got, new)
        x = new
        step *= radix
    return x


def sum_broadcast(x, axis, size):
    step = 1
    while step < size:
        perm = [(i, (i + step) % size) for i in range(size)]
        x = x + lax.ppermute(x, axis, perm)
        step *= 2
    return x


def window_perm(rows_count, cols_count):
    pairs = []
    for g in range(rows_count):
        for c2 in range(cols_count):
            r = c2 % rows_count
            c = g + rows_count * (c2 // rows_count)
            pairs.append((g * cols_count + c2, r * cols_count + c))
    return pairs


def kernel(left, right, left_index, right_index):
    left_sq = jnp.sum(left * left, axis=1)
    right_sq = jnp.sum(right * right, axis=1)
    cross = jnp.dot(
        left, right.T, precision=lax.Precision.HIGHEST, preferred_element_type=jnp.float32
    )
    dist_sq = jnp.maximum(left_sq[:, None] + right_sq[None, :] - 2.0 * cross, 0.0)
    radius = jnp.sqrt(dist_sq)
    value = (1.0 + root_five * radius + 5.0 / 3.0 * dist_sq) * jnp.exp(-root_five * radius)
    same = (left_index[:, None] == right_index[None, :]).astype(value.dtype)
    return value + noise_level * same


def factor_kernel(a_ref, low_ref, inv_ref):
    n = a_ref.shape[0]
    rows = lax.broadcasted_iota(jnp.int32, (n, n), 0)
    cols = lax.broadcasted_iota(jnp.int32, (n, n), 1)
    rcol = lax.broadcasted_iota(jnp.int32, (n, 1), 0)
    ccol = lax.broadcasted_iota(jnp.int32, (1, n), 1)
    m = a_ref[...]
    low = jnp.zeros((n, n), jnp.float32)
    inv = (rows == cols).astype(jnp.float32)
    for k in range(n):
        r = 1.0 / jnp.sqrt(m[k : k + 1, k : k + 1])
        lc = jnp.where(rcol >= k, m[:, k : k + 1] * r, 0.0)
        lr = jnp.where(ccol >= k, m[k : k + 1, :] * r, 0.0)
        m = m - lc * lr
        low = jnp.where(cols == k, lc, low)
        xk = inv[k : k + 1, :] * r
        inv = jnp.where(rows == k, xk, inv) - jnp.where(rcol > k, lc, 0.0) * xk
    low_ref[...] = low
    inv_ref[...] = inv


def factor_and_inverse(a):
    shape = jax.ShapeDtypeStruct(a.shape, jnp.float32)
    return pl.pallas_call(factor_kernel, out_shape=(shape, shape))(a)


def panel_solve(inverse, block):
    return jnp.dot(
        block, inverse.T, precision=lax.Precision.HIGHEST, preferred_element_type=jnp.float32
    )


def body(pool, row_pick, length_scale, panel_tile):
    rows_count = lax.axis_size("row")
    cols_count = lax.axis_size("col")
    my_row = lax.axis_index("row")
    my_col = lax.axis_index("col")
    total_rows = row_pick.shape[0]
    local_rows = total_rows // rows_count
    my_pick = lax.dynamic_slice_in_dim(row_pick, my_row * local_rows, local_rows)
    pool_rows = pool.shape[0]
    group_pixels = pool_rows * cols_count
    owner = my_pick // pool_rows
    owner_hot = (owner[:, None] == jnp.arange(cols_count)[None, :]).astype(jnp.bfloat16)
    pixel_hot = (my_pick[:, None] % pool_rows == jnp.arange(pool_rows)[None, :]).astype(jnp.bfloat16)
    picked = jnp.dot(owner_hot.T, pixel_hot, preferred_element_type=jnp.float32)
    counts = jnp.cumsum(picked, axis=1)
    mine = lax.dynamic_index_in_dim(counts, my_col, axis=0, keepdims=False)
    slots = jnp.arange(CAP, dtype=jnp.float32)
    local_idx = jnp.sum((mine[None, :] <= slots[:, None]).astype(jnp.int32), axis=1)
    compact = jnp.take(pool, jnp.minimum(local_idx, pool_rows - 1), axis=0)
    gathered = lax.all_gather(compact, "col", axis=0, tiled=True)
    row_counts = jnp.dot(owner_hot, counts.astype(jnp.bfloat16), preferred_element_type=jnp.float32)
    slot = jnp.sum(row_counts * pixel_hot.astype(jnp.float32), axis=1).astype(jnp.int32) - 1
    pick_idx = owner * CAP + slot
    panel = panel_tile[0]
    tiles = panel + 1 + jnp.mod(my_col - panel - 1, cols_count) + cols_count * jnp.arange(WT)
    served = my_row + rows_count * (my_col // rows_count)
    served_tiles = panel + 1 + jnp.mod(served - panel - 1, cols_count) + cols_count * jnp.arange(WT)
    local_tiles = served_tiles // rows_count
    col_source = (local_tiles[:, None] * TB + jnp.arange(TB)[None, :]).reshape(-1)
    all_rows = jnp.take(gathered, jnp.concatenate([pick_idx, jnp.take(pick_idx, col_source)]), axis=0)
    col_local = all_rows[local_rows:]
    col_feats = lax.ppermute(col_local, ("row", "col"), window_perm(rows_count, cols_count))
    panel_row = panel % rows_count
    panel_local = panel // rows_count
    panel_pick = lax.dynamic_slice_in_dim(row_pick, panel_row * local_rows + panel_local * TB, TB)
    held = (panel_pick // pool_rows == my_col) & (my_row == panel_row)
    panel_part = jnp.where(held[:, None], jnp.take(pool, panel_pick % pool_rows, axis=0), 0.0)
    panel_rows = sum_broadcast(sum_broadcast(panel_part, "col", cols_count), "row", rows_count)
    panel_feats = panel_rows
    features = all_rows[:local_rows]
    inverse_scale = 1.0 / length_scale
    scaled_rows = features * inverse_scale
    scaled_cols = col_feats * inverse_scale
    scaled_panel = panel_feats * inverse_scale
    local_index = jnp.arange(local_rows)
    row_global = (local_index // TB * rows_count + my_row) * TB + local_index % TB
    col_global = (tiles[:, None] * TB + jnp.arange(TB)[None, :]).reshape(-1)
    panel_global = panel * TB + jnp.arange(TB)
    factor, inverse = factor_and_inverse(kernel(scaled_panel, scaled_panel, panel_global, panel_global))
    row_panel = panel_solve(inverse, kernel(scaled_rows, scaled_panel, row_global, panel_global))
    col_panel = panel_solve(inverse, kernel(scaled_cols, scaled_panel, col_global, panel_global))
    update = jnp.dot(
        row_panel, col_panel.T, precision=lax.Precision.HIGHEST, preferred_element_type=jnp.float32
    )
    schur = kernel(scaled_rows, scaled_cols, row_global, col_global) - update
    return (schur, row_panel)


def solution(mesh):
    in_specs = (P(("row", "col"), None), P(), P(), P())
    out_specs = (P("row", "col"), P("row", None))
    return jax.shard_map(body, mesh=mesh, in_specs=in_specs, out_specs=out_specs, check_vma=False)
```

```python
import jax
import jax.numpy as jnp
from jax import lax
from jax.experimental import pallas as pl
from jax.sharding import PartitionSpec as P

TB = 64
WT = 2
CAP = 160


noise_level = 0.1
root_five = 5.0**0.5


def broadcast_rows(x, root, rows_count, radix=4):
    dist = jnp.mod(lax.axis_index("row") - root, rows_count)
    step = 1
    while step < rows_count:
        new = x
        for k in range(1, radix):
            shift = k * step
            if shift >= rows_count:
                break
            perm = [(i, (i + shift) % rows_count) for i in range(rows_count)]
            got = lax.ppermute(x, "row", perm)
            new = jnp.where((dist >= shift) & (dist < shift + step), got, new)
        x = new
        step *= radix
    return x


def sum_broadcast(x, axis, size):
    step = 1
    while step < size:
        perm = [(i, (i + step) % size) for i in range(size)]
        x = x + lax.ppermute(x, axis, perm)
        step *= 2
    return x


def window_perm(rows_count, cols_count):
    pairs = []
    for g in range(rows_count):
        for c2 in range(cols_count):
            r = c2 % rows_count
            c = g + rows_count * (c2 // rows_count)
            pairs.append((g * cols_count + c2, r * cols_count + c))
    return pairs


def kernel(left, right, left_index, right_index):
    left_sq = jnp.sum(left * left, axis=1)
    right_sq = jnp.sum(right * right, axis=1)
    cross = jnp.dot(
        left, right.T, precision=lax.Precision.HIGHEST, preferred_element_type=jnp.float32
    )
    dist_sq = jnp.maximum(left_sq[:, None] + right_sq[None, :] - 2.0 * cross, 0.0)
    radius = jnp.sqrt(dist_sq)
    value = (1.0 + root_five * radius + 5.0 / 3.0 * dist_sq) * jnp.exp(-root_five * radius)
    same = (left_index[:, None] == right_index[None, :]).astype(value.dtype)
    return value + noise_level * same


def factor_kernel(a_ref, low_ref, inv_ref):
    n = a_ref.shape[0]
    rows = lax.broadcasted_iota(jnp.int32, (n, n), 0)
    cols = lax.broadcasted_iota(jnp.int32, (n, n), 1)
    rcol = lax.broadcasted_iota(jnp.int32, (n, 1), 0)
    ccol = lax.broadcasted_iota(jnp.int32, (1, n), 1)
    m = a_ref[...]
    low = jnp.zeros((n, n), jnp.float32)
    inv = (rows == cols).astype(jnp.float32)
    for k in range(n):
        r = 1.0 / jnp.sqrt(m[k : k + 1, k : k + 1])
        lc = jnp.where(rcol >= k, m[:, k : k + 1] * r, 0.0)
        lr = jnp.where(ccol >= k, m[k : k + 1, :] * r, 0.0)
        m = m - lc * lr
        low = jnp.where(cols == k, lc, low)
        xk = inv[k : k + 1, :] * r
        inv = jnp.where(rows == k, xk, inv) - jnp.where(rcol > k, lc, 0.0) * xk
    low_ref[...] = low
    inv_ref[...] = inv


def factor_and_inverse(a):
    shape = jax.ShapeDtypeStruct(a.shape, jnp.float32)
    return pl.pallas_call(factor_kernel, out_shape=(shape, shape))(a)


def panel_solve(inverse, block):
    return jnp.dot(
        block, inverse.T, precision=lax.Precision.HIGHEST, preferred_element_type=jnp.float32
    )


def body(pool, row_pick, length_scale, panel_tile):
    rows_count = lax.axis_size("row")
    cols_count = lax.axis_size("col")
    my_row = lax.axis_index("row")
    my_col = lax.axis_index("col")
    total_rows = row_pick.shape[0]
    local_rows = total_rows // rows_count
    my_pick = lax.dynamic_slice_in_dim(row_pick, my_row * local_rows, local_rows)
    pool_rows = pool.shape[0]
    group_pixels = pool_rows * cols_count
    owner = my_pick // pool_rows
    owner_hot = (owner[:, None] == jnp.arange(cols_count)[None, :]).astype(jnp.bfloat16)
    pixel_hot = (my_pick[:, None] % pool_rows == jnp.arange(pool_rows)[None, :]).astype(jnp.bfloat16)
    picked = jnp.dot(owner_hot.T, pixel_hot, preferred_element_type=jnp.float32)
    counts = jnp.cumsum(picked, axis=1)
    mine = lax.dynamic_index_in_dim(counts, my_col, axis=0, keepdims=False)
    slots = jnp.arange(CAP, dtype=jnp.float32)
    local_idx = jnp.sum((mine[None, :] <= slots[:, None]).astype(jnp.int32), axis=1)
    compact = jnp.take(pool, jnp.minimum(local_idx, pool_rows - 1), axis=0)
    gathered = lax.all_gather(compact, "col", axis=0, tiled=True)
    row_counts = jnp.dot(owner_hot, counts.astype(jnp.bfloat16), preferred_element_type=jnp.float32)
    slot = jnp.sum(row_counts * pixel_hot.astype(jnp.float32), axis=1).astype(jnp.int32) - 1
    pick_idx = owner * CAP + slot
    panel = panel_tile[0]
    tiles = panel + 1 + jnp.mod(my_col - panel - 1, cols_count) + cols_count * jnp.arange(WT)
    served = my_row + rows_count * (my_col // rows_count)
    served_tiles = panel + 1 + jnp.mod(served - panel - 1, cols_count) + cols_count * jnp.arange(WT)
    local_tiles = served_tiles // rows_count
    col_source = (local_tiles[:, None] * TB + jnp.arange(TB)[None, :]).reshape(-1)
    all_rows = jnp.take(
        gathered, jnp.concatenate([pick_idx, jnp.take(pick_idx, col_source, mode="clip")]), axis=0, mode="clip"
    )
    col_local = all_rows[local_rows:]
    col_feats = lax.ppermute(col_local, ("row", "col"), window_perm(rows_count, cols_count))
    panel_row = panel % rows_count
    panel_local = panel // rows_count
    panel_pick = lax.dynamic_slice_in_dim(row_pick, panel_row * local_rows + panel_local * TB, TB)
    held = (panel_pick // pool_rows == my_col) & (my_row == panel_row)
    panel_part = jnp.where(held[:, None], jnp.take(pool, panel_pick % pool_rows, axis=0), 0.0)
    panel_rows = sum_broadcast(sum_broadcast(panel_part, "col", cols_count), "row", rows_count)
    panel_feats = panel_rows
    features = all_rows[:local_rows]
    inverse_scale = 1.0 / length_scale
    scaled_rows = features * inverse_scale
    scaled_cols = col_feats * inverse_scale
    scaled_panel = panel_feats * inverse_scale
    local_index = jnp.arange(local_rows)
    row_global = (local_index // TB * rows_count + my_row) * TB + local_index % TB
    col_global = (tiles[:, None] * TB + jnp.arange(TB)[None, :]).reshape(-1)
    panel_global = panel * TB + jnp.arange(TB)
    factor, inverse = factor_and_inverse(kernel(scaled_panel, scaled_panel, panel_global, panel_global))
    row_panel = panel_solve(inverse, kernel(scaled_rows, scaled_panel, row_global, panel_global))
    col_panel = panel_solve(inverse, kernel(scaled_cols, scaled_panel, col_global, panel_global))
    update = jnp.dot(
        row_panel, col_panel.T, precision=lax.Precision.HIGHEST, preferred_element_type=jnp.float32
    )
    schur = kernel(scaled_rows, scaled_cols, row_global, col_global) - update
    return (schur, row_panel)


def solution(mesh):
    in_specs = (P(("row", "col"), None), P(), P(), P())
    out_specs = (P("row", "col"), P("row", None))
    return jax.shard_map(body, mesh=mesh, in_specs=in_specs, out_specs=out_specs, check_vma=False)
```

```python
import jax
import jax.numpy as jnp
from jax import lax
from jax.experimental import pallas as pl
from jax.sharding import PartitionSpec as P

TB = 64
WT = 2
CAP = 160


noise_level = 0.1
root_five = 5.0**0.5


def broadcast_rows(x, root, rows_count, radix=4):
    dist = jnp.mod(lax.axis_index("row") - root, rows_count)
    step = 1
    while step < rows_count:
        new = x
        for k in range(1, radix):
            shift = k * step
            if shift >= rows_count:
                break
            perm = [(i, (i + shift) % rows_count) for i in range(rows_count)]
            got = lax.ppermute(x, "row", perm)
            new = jnp.where((dist >= shift) & (dist < shift + step), got, new)
        x = new
        step *= radix
    return x


def sum_broadcast(x, axis, size):
    step = 1
    while step < size:
        perm = [(i, (i + step) % size) for i in range(size)]
        x = x + lax.ppermute(x, axis, perm)
        step *= 2
    return x


def window_perm(rows_count, cols_count):
    pairs = []
    for g in range(rows_count):
        for c2 in range(cols_count):
            r = c2 % rows_count
            c = g + rows_count * (c2 // rows_count)
            pairs.append((g * cols_count + c2, r * cols_count + c))
    return pairs


def kernel(left, right, left_index, right_index):
    left_sq = jnp.sum(left * left, axis=1)
    right_sq = jnp.sum(right * right, axis=1)
    cross = jnp.dot(
        left, right.T, precision=lax.Precision.HIGHEST, preferred_element_type=jnp.float32
    )
    dist_sq = jnp.maximum(left_sq[:, None] + right_sq[None, :] - 2.0 * cross, 0.0)
    radius = jnp.sqrt(dist_sq)
    value = (1.0 + root_five * radius + 5.0 / 3.0 * dist_sq) * jnp.exp(-root_five * radius)
    same = (left_index[:, None] == right_index[None, :]).astype(value.dtype)
    return value + noise_level * same


def factor_kernel(a_ref, low_ref, inv_ref):
    n = a_ref.shape[0]
    rows = lax.broadcasted_iota(jnp.int32, (n, n), 0)
    cols = lax.broadcasted_iota(jnp.int32, (n, n), 1)
    rcol = lax.broadcasted_iota(jnp.int32, (n, 1), 0)
    ccol = lax.broadcasted_iota(jnp.int32, (1, n), 1)
    m = a_ref[...]
    low = jnp.zeros((n, n), jnp.float32)
    inv = (rows == cols).astype(jnp.float32)
    for k in range(n):
        r = 1.0 / jnp.sqrt(m[k : k + 1, k : k + 1])
        lc = jnp.where(rcol >= k, m[:, k : k + 1] * r, 0.0)
        lr = jnp.where(ccol >= k, m[k : k + 1, :] * r, 0.0)
        m = m - lc * lr
        low = jnp.where(cols == k, lc, low)
        xk = inv[k : k + 1, :] * r
        inv = jnp.where(rows == k, xk, inv) - jnp.where(rcol > k, lc, 0.0) * xk
    low_ref[...] = low
    inv_ref[...] = inv


def factor_and_inverse(a):
    shape = jax.ShapeDtypeStruct(a.shape, jnp.float32)
    return pl.pallas_call(factor_kernel, out_shape=(shape, shape))(a)


def panel_solve(inverse, block):
    return jnp.dot(
        block, inverse.T, precision=lax.Precision.HIGHEST, preferred_element_type=jnp.float32
    )


def body(pool, row_pick, length_scale, panel_tile):
    rows_count = lax.axis_size("row")
    cols_count = lax.axis_size("col")
    my_row = lax.axis_index("row")
    my_col = lax.axis_index("col")
    total_rows = row_pick.shape[0]
    local_rows = total_rows // rows_count
    my_pick = lax.dynamic_slice_in_dim(row_pick, my_row * local_rows, local_rows)
    pool_rows = pool.shape[0]
    group_pixels = pool_rows * cols_count
    owner = my_pick // pool_rows
    owner_hot = (owner[:, None] == jnp.arange(cols_count)[None, :]).astype(jnp.bfloat16)
    pixel_hot = (my_pick[:, None] % pool_rows == jnp.arange(pool_rows)[None, :]).astype(jnp.bfloat16)
    picked = jnp.dot(owner_hot.T, pixel_hot, preferred_element_type=jnp.float32)
    counts = jnp.cumsum(picked, axis=1)
    mine = lax.dynamic_index_in_dim(counts, my_col, axis=0, keepdims=False)
    slots = jnp.arange(CAP, dtype=jnp.float32)
    local_idx = jnp.sum((mine[None, :] <= slots[:, None]).astype(jnp.int32), axis=1)
    compact = jnp.take(pool, jnp.minimum(local_idx, pool_rows - 1), axis=0, mode="clip")
    gathered = lax.all_gather(compact, "col", axis=0, tiled=True)
    row_counts = jnp.dot(owner_hot, counts.astype(jnp.bfloat16), preferred_element_type=jnp.float32)
    slot = jnp.sum(row_counts * pixel_hot.astype(jnp.float32), axis=1).astype(jnp.int32) - 1
    pick_idx = owner * CAP + slot
    panel = panel_tile[0]
    tiles = panel + 1 + jnp.mod(my_col - panel - 1, cols_count) + cols_count * jnp.arange(WT)
    served = my_row + rows_count * (my_col // rows_count)
    served_tiles = panel + 1 + jnp.mod(served - panel - 1, cols_count) + cols_count * jnp.arange(WT)
    local_tiles = served_tiles // rows_count
    col_source = (local_tiles[:, None] * TB + jnp.arange(TB)[None, :]).reshape(-1)
    all_rows = jnp.take(gathered, jnp.concatenate([pick_idx, jnp.take(pick_idx, col_source)]), axis=0)
    col_local = all_rows[local_rows:]
    col_feats = lax.ppermute(col_local, ("row", "col"), window_perm(rows_count, cols_count))
    panel_row = panel % rows_count
    panel_local = panel // rows_count
    panel_pick = lax.dynamic_slice_in_dim(row_pick, panel_row * local_rows + panel_local * TB, TB)
    held = (panel_pick // pool_rows == my_col) & (my_row == panel_row)
    panel_part = jnp.where(held[:, None], jnp.take(pool, panel_pick % pool_rows, axis=0), 0.0)
    panel_rows = sum_broadcast(sum_broadcast(panel_part, "col", cols_count), "row", rows_count)
    panel_feats = panel_rows
    features = all_rows[:local_rows]
    inverse_scale = 1.0 / length_scale
    scaled_rows = features * inverse_scale
    scaled_cols = col_feats * inverse_scale
    scaled_panel = panel_feats * inverse_scale
    local_index = jnp.arange(local_rows)
    row_global = (local_index // TB * rows_count + my_row) * TB + local_index % TB
    col_global = (tiles[:, None] * TB + jnp.arange(TB)[None, :]).reshape(-1)
    panel_global = panel * TB + jnp.arange(TB)
    factor, inverse = factor_and_inverse(kernel(scaled_panel, scaled_panel, panel_global, panel_global))
    row_panel = panel_solve(inverse, kernel(scaled_rows, scaled_panel, row_global, panel_global))
    col_panel = panel_solve(inverse, kernel(scaled_cols, scaled_panel, col_global, panel_global))
    update = jnp.dot(
        row_panel, col_panel.T, precision=lax.Precision.HIGHEST, preferred_element_type=jnp.float32
    )
    schur = kernel(scaled_rows, scaled_cols, row_global, col_global) - update
    return (schur, row_panel)


def solution(mesh):
    in_specs = (P(("row", "col"), None), P(), P(), P())
    out_specs = (P("row", "col"), P("row", None))
    return jax.shard_map(body, mesh=mesh, in_specs=in_specs, out_specs=out_specs, check_vma=False)
```

```python
import jax
import jax.numpy as jnp
from jax import lax
from jax.experimental import pallas as pl
from jax.sharding import PartitionSpec as P

TB = 64
WT = 2
CAP = 160


noise_level = 0.1
root_five = 5.0**0.5


def broadcast_rows(x, root, rows_count, radix=4):
    dist = jnp.mod(lax.axis_index("row") - root, rows_count)
    step = 1
    while step < rows_count:
        new = x
        for k in range(1, radix):
            shift = k * step
            if shift >= rows_count:
                break
            perm = [(i, (i + shift) % rows_count) for i in range(rows_count)]
            got = lax.ppermute(x, "row", perm)
            new = jnp.where((dist >= shift) & (dist < shift + step), got, new)
        x = new
        step *= radix
    return x


def sum_broadcast(x, axis, size):
    step = 1
    while step < size:
        perm = [(i, (i + step) % size) for i in range(size)]
        x = x + lax.ppermute(x, axis, perm)
        step *= 2
    return x


def window_perm(rows_count, cols_count):
    pairs = []
    for g in range(rows_count):
        for c2 in range(cols_count):
            r = c2 % rows_count
            c = g + rows_count * (c2 // rows_count)
            pairs.append((g * cols_count + c2, r * cols_count + c))
    return pairs


def kernel(left, right, left_index, right_index):
    left_sq = jnp.sum(left * left, axis=1)
    right_sq = jnp.sum(right * right, axis=1)
    cross = jnp.dot(
        left, right.T, precision=lax.Precision.HIGHEST, preferred_element_type=jnp.float32
    )
    dist_sq = jnp.maximum(left_sq[:, None] + right_sq[None, :] - 2.0 * cross, 0.0)
    radius = jnp.sqrt(dist_sq)
    value = (1.0 + root_five * radius + 5.0 / 3.0 * dist_sq) * jnp.exp(-root_five * radius)
    same = (left_index[:, None] == right_index[None, :]).astype(value.dtype)
    return value + noise_level * same


def factor_kernel(a_ref, low_ref, inv_ref):
    n = a_ref.shape[0]
    rows = lax.broadcasted_iota(jnp.int32, (n, n), 0)
    cols = lax.broadcasted_iota(jnp.int32, (n, n), 1)
    rcol = lax.broadcasted_iota(jnp.int32, (n, 1), 0)
    ccol = lax.broadcasted_iota(jnp.int32, (1, n), 1)
    m = a_ref[...]
    low = jnp.zeros((n, n), jnp.float32)
    inv = (rows == cols).astype(jnp.float32)
    for k in range(n):
        r = 1.0 / jnp.sqrt(m[k : k + 1, k : k + 1])
        lc = jnp.where(rcol >= k, m[:, k : k + 1] * r, 0.0)
        lr = jnp.where(ccol >= k, m[k : k + 1, :] * r, 0.0)
        m = m - lc * lr
        low = jnp.where(cols == k, lc, low)
        xk = inv[k : k + 1, :] * r
        inv = jnp.where(rows == k, xk, inv) - jnp.where(rcol > k, lc, 0.0) * xk
    low_ref[...] = low
    inv_ref[...] = inv


def factor_and_inverse(a):
    shape = jax.ShapeDtypeStruct(a.shape, jnp.float32)
    return pl.pallas_call(factor_kernel, out_shape=(shape, shape))(a)


def panel_solve(inverse, block):
    return jnp.dot(
        block, inverse.T, precision=lax.Precision.HIGHEST, preferred_element_type=jnp.float32
    )


def body(pool, row_pick, length_scale, panel_tile):
    rows_count = lax.axis_size("row")
    cols_count = lax.axis_size("col")
    my_row = lax.axis_index("row")
    my_col = lax.axis_index("col")
    total_rows = row_pick.shape[0]
    local_rows = total_rows // rows_count
    my_pick = lax.dynamic_slice_in_dim(row_pick, my_row * local_rows, local_rows)
    pool_rows = pool.shape[0]
    group_pixels = pool_rows * cols_count
    owner = my_pick // pool_rows
    owner_hot = (owner[:, None] == jnp.arange(cols_count)[None, :]).astype(jnp.bfloat16)
    pixel_hot = (my_pick[:, None] % pool_rows == jnp.arange(pool_rows)[None, :]).astype(jnp.bfloat16)
    picked = jnp.dot(owner_hot.T, pixel_hot, preferred_element_type=jnp.float32)
    upper = (jnp.arange(pool_rows)[:, None] <= jnp.arange(pool_rows)[None, :]).astype(jnp.bfloat16)
    counts = jnp.dot(picked.astype(jnp.bfloat16), upper, preferred_element_type=jnp.float32)
    mine = lax.dynamic_index_in_dim(counts, my_col, axis=0, keepdims=False)
    slots = jnp.arange(CAP, dtype=jnp.float32)
    local_idx = jnp.sum((mine[None, :] <= slots[:, None]).astype(jnp.int32), axis=1)
    compact = jnp.take(pool, jnp.minimum(local_idx, pool_rows - 1), axis=0)
    gathered = lax.all_gather(compact, "col", axis=0, tiled=True)
    row_counts = jnp.dot(owner_hot, counts.astype(jnp.bfloat16), preferred_element_type=jnp.float32)
    slot = jnp.sum(row_counts * pixel_hot.astype(jnp.float32), axis=1).astype(jnp.int32) - 1
    pick_idx = owner * CAP + slot
    panel = panel_tile[0]
    tiles = panel + 1 + jnp.mod(my_col - panel - 1, cols_count) + cols_count * jnp.arange(WT)
    served = my_row + rows_count * (my_col // rows_count)
    served_tiles = panel + 1 + jnp.mod(served - panel - 1, cols_count) + cols_count * jnp.arange(WT)
    local_tiles = served_tiles // rows_count
    col_source = (local_tiles[:, None] * TB + jnp.arange(TB)[None, :]).reshape(-1)
    all_rows = jnp.take(gathered, jnp.concatenate([pick_idx, jnp.take(pick_idx, col_source)]), axis=0)
    col_local = all_rows[local_rows:]
    col_feats = lax.ppermute(col_local, ("row", "col"), window_perm(rows_count, cols_count))
    panel_row = panel % rows_count
    panel_local = panel // rows_count
    panel_pick = lax.dynamic_slice_in_dim(row_pick, panel_row * local_rows + panel_local * TB, TB)
    held = (panel_pick // pool_rows == my_col) & (my_row == panel_row)
    panel_part = jnp.where(held[:, None], jnp.take(pool, panel_pick % pool_rows, axis=0), 0.0)
    panel_rows = sum_broadcast(sum_broadcast(panel_part, "col", cols_count), "row", rows_count)
    panel_feats = panel_rows
    features = all_rows[:local_rows]
    inverse_scale = 1.0 / length_scale
    scaled_rows = features * inverse_scale
    scaled_cols = col_feats * inverse_scale
    scaled_panel = panel_feats * inverse_scale
    local_index = jnp.arange(local_rows)
    row_global = (local_index // TB * rows_count + my_row) * TB + local_index % TB
    col_global = (tiles[:, None] * TB + jnp.arange(TB)[None, :]).reshape(-1)
    panel_global = panel * TB + jnp.arange(TB)
    factor, inverse = factor_and_inverse(kernel(scaled_panel, scaled_panel, panel_global, panel_global))
    row_panel = panel_solve(inverse, kernel(scaled_rows, scaled_panel, row_global, panel_global))
    col_panel = panel_solve(inverse, kernel(scaled_cols, scaled_panel, col_global, panel_global))
    update = jnp.dot(
        row_panel, col_panel.T, precision=lax.Precision.HIGHEST, preferred_element_type=jnp.float32
    )
    schur = kernel(scaled_rows, scaled_cols, row_global, col_global) - update
    return (schur, row_panel)


def solution(mesh):
    in_specs = (P(("row", "col"), None), P(), P(), P())
    out_specs = (P("row", "col"), P("row", None))
    return jax.shard_map(body, mesh=mesh, in_specs=in_specs, out_specs=out_specs, check_vma=False)
```
